128 devices in a mesh: tok: 32 (over z, x, core), head: 4 (over y).
Axes of the slice: x: 4, y: 4, z: 4, core: 2. Of those that a mesh axis runs over, the one named last changes fastest.
Arguments:
- hidden_in: bfloat16 [32, 512, 5120], P('tok', None, 'head')
- norm_gain: float32 [5120], replicated, may hold values from 0.1 to 1.9
- w_query: bfloat16 [5120, 2048], P(None, 'head'), may hold values from -0.078125 to 0.078125
- w_key: bfloat16 [5120, 512], P(None, 'head'), may hold values from -0.15625 to 0.15625
- w_value: bfloat16 [5120, 512], P(None, 'head'), may hold values from -0.078125 to 0.078125
- w_out: bfloat16 [2048, 5120], P(None, 'head'), may hold values from -0.5 to 0.5
- prefix_cache: bfloat16 [64, 2, 128, 512], P('tok', None, None, 'head')
- suffix_len: int32 [32], replicated, may hold values from 1 to 512, 10240 in all
- page_table: int32 [2, 32], replicated, may hold values from 0 to 63, as said below
- request_group: int32 [32], replicated, may hold values from 0 to 1, as said below
Outputs:
- hidden_out: bfloat16 [32, 512, 5120], P('tok', None, 'head')
The draws below stay inside these ranges and needn't reach their ends.
Inputs may be any that keep to these rules, and one draw needn't show every extreme that they name: `page_table`: every one of the 64 slots appears exactly once; row g lists the slots that hold group g's prefix pages, page by page. `request_group`: exactly half of the 32 requests are in each group.
All inputs are finite; a program needn't handle non-finite values.
Results may differ from the reference program's by a relative error of at most 0.008.
The reference program's roundings to bfloat16 on the way count: a program that leaves them out, or rounds other values in their place, can miss the bound.
Values may be sent and summed in bfloat16 or wider, within the bound.
No kernel may reach another device: no remote copies, remote signals or barrier semaphores. Data moves between devices by JAX's collectives and lax.ppermute only.
A program may use at most 128 MiB of HBM per device.

```python
import math
import jax
import jax.numpy as jnp
import numpy as np
from jax import lax

D = 5120
HEADS = 16
KVH = 4
HD = 128
PAGE = 128
SUF = 512
PREFIX = 4096
QH = 4
REQS = 32
PAGES = 64


def draw_hidden_in(key, part):
    noise_key, row_key, column_key = jax.random.split(key, 3)
    shape = (REQS, SUF, D)
    base = jax.random.normal(noise_key, shape, jnp.float32)
    row_scale = jnp.exp(jax.random.uniform(row_key, (REQS, SUF, 1), jnp.float32, 0.0, 2.3))
    column_scale = jnp.exp(jax.random.uniform(column_key, (1, 1, D), jnp.float32, -0.7, 0.7))
    return (base * row_scale * column_scale).astype(jnp.bfloat16)


def draw_prefix_cache(key, part):
    split_keys = jax.random.split(key, 1)
    cache = jax.random.normal(split_keys[0], (PAGES, 2, PAGE, KVH * HD), jnp.float32)
    return cache.astype(jnp.bfloat16)


def draw_page_table(key, part):
    order = jax.random.permutation(jax.random.fold_in(key, 11), PAGES)
    return order.astype(jnp.int32).reshape(2, PAGES // 2)


def draw_request_group(key, part):
    order = jax.random.permutation(jax.random.fold_in(key, 23), REQS)
    return (order >= REQS // 2).astype(jnp.int32)


def levels(own_key, shape, cuts, low, high):
    loudness = 1.0
    for axis_at, blocks in cuts:
        draws = jax.random.uniform(jax.random.fold_in(jax.random.fold_in(own_key, 6), axis_at), (blocks,), jnp.float32, low / len(cuts), high / len(cuts))
        loudness = loudness * jnp.repeat(jnp.exp(draws), shape[axis_at] // blocks).reshape((-1,) + (1,) * (len(shape) - 1 - axis_at))
    return loudness


def split_up(amount, total, most, lean):
    weights = [(1 << 20) // math.isqrt(standing ** lean) + 1 for standing in range(2, amount + 1)]
    rest, holding = total - most - (amount - 1), [1] * (amount - 1)
    while rest > 0:
        candidates = [i for i in range(amount - 1) if holding[i] < most]
        mass, budget = sum([weights[i] for i in candidates]), rest
        for i in candidates:
            extra = min(most - holding[i], max(1, budget * weights[i] // mass), rest)
            holding[i] = holding[i] + extra
            rest = rest - extra
    return np.array([most] + holding)


def uneven_parts(stream_key, count, total, limit, slope):
    if count == 2:
        one = jax.random.randint(stream_key, (), max(1, total - limit), min(limit, total - 1) + 1)
        return jnp.stack([one, total - one])
    tallies = jnp.asarray(split_up(count, total, limit, slope), jnp.int32)
    pairs = (count - 1) // 2
    source_of, taker = tallies[1:1 + 2 * pairs:2], tallies[2:2 + 2 * pairs:2]
    margin = jnp.minimum(source_of - 1, limit - taker)
    shifted = jax.random.randint(jax.random.fold_in(stream_key, 1), (pairs,), 0, 1 << 20) % (margin + 1)
    tallies = tallies.at[1:1 + 2 * pairs:2].set(source_of - shifted).at[2:2 + 2 * pairs:2].set(taker + shifted)
    return tallies[jax.random.permutation(jax.random.fold_in(stream_key, 2), count)]


def normal_values(rng, extent, spread, bound, cuts=(), kind=jnp.bfloat16):
    values = jax.random.normal(rng, extent, jnp.float32) * spread
    if len(cuts) > 0:
        values = levels(rng, extent, cuts, -0.22, 0.18) * values
    return jnp.clip(values, min=-bound, max=bound).astype(kind)


def setup_inputs(seed: int = 0) -> dict:
    key_of = jax.random.split(jax.random.key(seed), 11)
    return {
        "hidden_in": draw_hidden_in(jax.random.fold_in(key_of[10], 71), 0),
        "norm_gain": jnp.clip(1.0 + 0.18 * jax.random.normal(key_of[1], (D,), jnp.float32), 0.1, 1.9),
        "w_query": normal_values(key_of[2], (D, HEADS * HD), D ** -0.5, 0.078125, ((1, 4),)),
        "w_key": normal_values(key_of[3], (D, KVH * HD), (D // 4) ** -0.5, 0.15625, ((1, 4),)),
        "w_value": normal_values(key_of[4], (D, KVH * HD), D ** -0.5, 0.078125, ((1, 4),)),
        "w_out": normal_values(key_of[5], (HEADS * HD, D), HD ** -0.5, 0.5, ((1, 4),)),
        "prefix_cache": draw_prefix_cache(jax.random.fold_in(key_of[10], 71), 0),
        "suffix_len": uneven_parts(key_of[7], REQS, REQS * SUF * 5 // 8, SUF, 1).astype(jnp.int32),
        "page_table": draw_page_table(jax.random.fold_in(key_of[10], 71), 0),
        "request_group": draw_request_group(jax.random.fold_in(key_of[10], 71), 0),
    }


THETA = 100000000.0
EPS = 1e-05
NEG = -1e+30

def rope_angles(positions, size):
    half = size // 2
    ladder = jnp.arange(half, dtype=jnp.float32)
    freq = jnp.exp(ladder * (-2.0 * jnp.log(THETA) / size))
    angle = positions.astype(jnp.float32)[:, None] * freq[None, :]
    return (jnp.cos(angle), jnp.sin(angle))

def rotate(values, cosine, sine):
    half = values.shape[-1] // 2
    first = values[..., :half]
    second = values[..., half:]
    return jnp.concatenate([first * cosine - second * sine, second * cosine + first * sine], axis=-1)

def reference(hidden_in, norm_gain, w_query, w_key, w_value, w_out, prefix_cache, suffix_len, page_table, request_group):
    rows = hidden_in.reshape(REQS * SUF, D).astype(jnp.float32)
    inverse = lax.rsqrt(lax.optimization_barrier(jnp.mean(rows * rows, axis=1, keepdims=True)) + EPS)
    normed = (rows * inverse * norm_gain[None, :]).astype(jnp.bfloat16)
    cosine, sine = rope_angles(PREFIX + jnp.arange(SUF, dtype=jnp.int32), HD)
    cosine = cosine[None, :, None, :]
    sine = sine[None, :, None, :]
    query = jnp.dot(normed, w_query, preferred_element_type=jnp.float32).reshape(REQS, SUF, HEADS, HD)
    query = rotate(query, cosine, sine).astype(jnp.bfloat16)
    keys = jnp.dot(normed, w_key, preferred_element_type=jnp.float32).reshape(REQS, SUF, KVH, HD)
    keys = rotate(keys, cosine, sine).astype(jnp.bfloat16)
    values = jnp.dot(normed, w_value, preferred_element_type=jnp.float32).astype(jnp.bfloat16).reshape(REQS, SUF, KVH, HD)
    position = jnp.arange(SUF, dtype=jnp.int32)

    def attend(items):
        query_one, keys_one, values_one, length, group = items
        cache = jnp.take(prefix_cache, page_table[group], axis=0)
        cache_keys = cache[:, 0].reshape(PREFIX, KVH, HD)
        cache_values = cache[:, 1].reshape(PREFIX, KVH, HD)
        all_keys = jnp.concatenate([cache_keys, keys_one], axis=0).astype(jnp.float32)
        all_values = jnp.concatenate([cache_values, values_one], axis=0).astype(jnp.float32)
        grouped = query_one.reshape(SUF, KVH, QH, HD).astype(jnp.float32)
        scores = jnp.einsum('sgqd,tgd->gqst', grouped, all_keys) * HD ** (-0.5)
        causal = (position[None, :] <= position[:, None]) & (position[None, :] < length)
        allowed = jnp.concatenate([jnp.ones((SUF, PREFIX), dtype=bool), causal], axis=1)
        scores = jnp.where(allowed, scores, NEG)
        highest = lax.optimization_barrier(jnp.max(scores, axis=-1, keepdims=True))
        weights = jnp.where(allowed, jnp.exp(scores - highest), 0.0)
        total = lax.optimization_barrier(jnp.sum(weights, axis=-1, keepdims=True))
        rounded = lax.optimization_barrier(weights.astype(jnp.bfloat16)).astype(jnp.float32)
        mixed = jnp.einsum('gqst,tgd->gqsd', rounded, all_values) / total
        return mixed.astype(jnp.bfloat16).transpose(2, 0, 1, 3).reshape(SUF, HEADS * HD)
    attention = lax.map(attend, (query, keys, values, suffix_len, request_group))
    output = jnp.dot(attention.reshape(REQS * SUF, HEADS * HD), w_out, preferred_element_type=jnp.float32)
    output = output.reshape(REQS, SUF, D)
    live = position[None, :] < suffix_len[:, None]
    return jnp.where(live[:, :, None], output, 0.0).astype(jnp.bfloat16)
```

```python
import functools
import os

import jax
import jax.numpy as jnp
from jax import lax
from jax.experimental import pallas as pl
from jax.experimental.pallas import tpu as pltpu
from jax.sharding import PartitionSpec as P

HD = 128
PREFIX = 4096


THETA = 100000000.0
EPS = 1e-05
NEG = -1e30
TQ = 256
INTERPRET = os.environ.get("SOL_INTERPRET") == "1"


def rope_angles(positions, size):
    half = size // 2
    ladder = jnp.arange(half, dtype=jnp.float32)
    freq = jnp.exp(ladder * (-2.0 * jnp.log(THETA) / size))
    angle = positions.astype(jnp.float32)[:, None] * freq[None, :]
    return (jnp.cos(angle), jnp.sin(angle))


def rotate(values, cosine, sine):
    half = values.shape[-1] // 2
    first = values[..., :half]
    second = values[..., half:]
    return jnp.concatenate(
        [first * cosine - second * sine, second * cosine + first * sine], axis=-1
    )


def attention_kernel(len_ref, q_ref, kp_ref, vp_ref, ks_ref, vs_ref, o_ref):
    i = pl.program_id(1)
    length = len_ref[0]
    q = q_ref[...]
    scale = HD ** (-0.5)
    dims = (((1,), (1,)), ((), ()))
    sp = lax.dot_general(q, kp_ref[...], dims, preferred_element_type=jnp.float32) * scale
    ss = lax.dot_general(q, ks_ref[...], dims, preferred_element_type=jnp.float32) * scale
    rows, cols = ss.shape
    qpos = i * rows + lax.broadcasted_iota(jnp.int32, (rows, cols), 0)
    kpos = lax.broadcasted_iota(jnp.int32, (rows, cols), 1)
    allowed = (kpos <= qpos) & (kpos < length)
    ss = jnp.where(allowed, ss, NEG)
    high = jnp.maximum(jnp.max(sp, axis=1, keepdims=True), jnp.max(ss, axis=1, keepdims=True))
    wp = jnp.exp(sp - high)
    ws = jnp.where(allowed, jnp.exp(ss - high), 0.0)
    total = jnp.sum(wp, axis=1, keepdims=True) + jnp.sum(ws, axis=1, keepdims=True)
    acc = jnp.dot(wp.astype(jnp.bfloat16), vp_ref[...], preferred_element_type=jnp.float32)
    acc = acc + jnp.dot(ws.astype(jnp.bfloat16), vs_ref[...], preferred_element_type=jnp.float32)
    o_ref[...] = (acc / total).astype(o_ref.dtype)


def attend(length, query, kp, vp, ks, vs, per_kv):
    local_len = query.shape[0]
    nq = local_len // TQ
    grid_spec = pltpu.PrefetchScalarGridSpec(
        num_scalar_prefetch=1,
        grid=(per_kv, nq),
        in_specs=[
            pl.BlockSpec((TQ, HD), lambda j, i, n: (i, j)),
            pl.BlockSpec(kp.shape, lambda j, i, n: (0, 0)),
            pl.BlockSpec(vp.shape, lambda j, i, n: (0, 0)),
            pl.BlockSpec(ks.shape, lambda j, i, n: (0, 0)),
            pl.BlockSpec(vs.shape, lambda j, i, n: (0, 0)),
        ],
        out_specs=pl.BlockSpec((TQ, HD), lambda j, i, n: (i, j)),
    )
    return pl.pallas_call(
        attention_kernel,
        grid_spec=grid_spec,
        out_shape=jax.ShapeDtypeStruct((local_len, per_kv * HD), jnp.bfloat16),
        compiler_params=pltpu.CompilerParams(vmem_limit_bytes=48 * 1024 * 1024),
        interpret=INTERPRET,
    )(length.reshape(1), query, kp, vp, ks, vs)


def local(
    hidden_in,
    norm_gain,
    w_query,
    w_key,
    w_value,
    w_out,
    prefix_cache,
    suffix_len,
    page_table,
    request_group,
):
    n_head = lax.axis_size("head")
    me = lax.axis_index("head")
    device = lax.axis_index("tok")
    local_len = hidden_in.shape[1]
    feat = hidden_in.shape[2]
    width = feat * n_head
    piece = lax.all_gather(prefix_cache, "tok", axis=0, tiled=True)

    x = hidden_in.reshape(local_len, feat)
    xf = x.astype(jnp.float32)
    own_ss = jnp.sum(xf * xf, axis=1)
    blocks = [(0, x, own_ss)]
    for s in range(1, n_head):
        perm = [(j, (j + s) % n_head) for j in range(n_head)]
        blocks.append((s, lax.ppermute(x, "head", perm), lax.ppermute(own_ss, "head", perm)))
    total_ss = blocks[0][2]
    for b in blocks[1:]:
        total_ss = total_ss + b[2]
    inverse = lax.rsqrt(total_ss / width + EPS)[:, None]

    head_size = HD
    kv_local = w_key.shape[1] // head_size
    q_local = w_query.shape[1] // head_size
    per_kv = q_local // kv_local
    proj_q = proj_k = proj_v = None
    for s, xb, _ in blocks:
        src = (me - s) % n_head
        gain = lax.dynamic_slice_in_dim(norm_gain, src * feat, feat)
        nb = (xb.astype(jnp.float32) * inverse * gain[None, :]).astype(jnp.bfloat16)
        pq = jnp.dot(nb, lax.dynamic_slice_in_dim(w_query, src * feat, feat, 0),
                     preferred_element_type=jnp.float32)
        pk = jnp.dot(nb, lax.dynamic_slice_in_dim(w_key, src * feat, feat, 0),
                     preferred_element_type=jnp.float32)
        pv = jnp.dot(nb, lax.dynamic_slice_in_dim(w_value, src * feat, feat, 0),
                     preferred_element_type=jnp.float32)
        if proj_q is None:
            proj_q, proj_k, proj_v = pq, pk, pv
        else:
            proj_q, proj_k, proj_v = proj_q + pq, proj_k + pk, proj_v + pv

    positions = PREFIX + jnp.arange(local_len, dtype=jnp.int32)
    cosine, sine = rope_angles(positions, head_size)
    cosine = cosine[:, None, :]
    sine = sine[:, None, :]
    query = rotate(proj_q.reshape(local_len, q_local, head_size), cosine, sine)
    query = query.astype(jnp.bfloat16).reshape(local_len, q_local * head_size)
    keys = rotate(proj_k.reshape(local_len, kv_local, head_size), cosine, sine)
    keys = keys.astype(jnp.bfloat16).reshape(local_len, kv_local * head_size)
    values = proj_v.astype(jnp.bfloat16)

    length = suffix_len[device]
    group = request_group[device]
    own_pages = page_table[group]
    chosen = jnp.take(piece, own_pages, axis=0)
    kp = chosen[:, 0].reshape(-1, head_size)
    vp = chosen[:, 1].reshape(-1, head_size)
    mixed = attend(length, query, kp, vp, keys, values, per_kv)

    rows_per = mixed.shape[1]
    output = None
    for s in range(n_head):
        if s == 0:
            part = mixed
        else:
            perm = [(j, (j + s) % n_head) for j in range(n_head)]
            part = lax.ppermute(mixed, "head", perm)
        src = (me - s) % n_head
        w_rows = lax.dynamic_slice_in_dim(w_out, src * rows_per, rows_per, 0)
        po = jnp.dot(part, w_rows, preferred_element_type=jnp.float32)
        output = po if output is None else output + po
    live = jnp.arange(local_len, dtype=jnp.int32) < length
    output = jnp.where(live[:, None], output, 0.0).astype(jnp.bfloat16)
    return output.reshape(1, local_len, w_out.shape[1])


def solution(mesh):
    return jax.shard_map(
        local,
        mesh=mesh,
        in_specs=(
            P("tok", None, "head"),
            P(),
            P(None, "head"),
            P(None, "head"),
            P(None, "head"),
            P(None, "head"),
            P("tok", None, None, "head"),
            P(),
            P(),
            P(),
        ),
        out_specs=P("tok", None, "head"),
        check_vma=False,
    )
```

```python
import functools
import os

import jax
import jax.numpy as jnp
from jax import lax
from jax.experimental import pallas as pl
from jax.experimental.pallas import tpu as pltpu
from jax.sharding import PartitionSpec as P

HD = 128
PREFIX = 4096


THETA = 100000000.0
EPS = 1e-05
NEG = -1e30
CHUNKS = 4
INTERPRET = os.environ.get("SOL_INTERPRET") == "1"


def rope_angles(positions, size):
    half = size // 2
    ladder = jnp.arange(half, dtype=jnp.float32)
    freq = jnp.exp(ladder * (-2.0 * jnp.log(THETA) / size))
    angle = positions.astype(jnp.float32)[:, None] * freq[None, :]
    return (jnp.cos(angle), jnp.sin(angle))


def rotate(values, cosine, sine):
    half = values.shape[-1] // 2
    first = values[..., :half]
    second = values[..., half:]
    return jnp.concatenate(
        [first * cosine - second * sine, second * cosine + first * sine], axis=-1
    )


def attention_kernel(len_ref, q_ref, kp_ref, vp_ref, ks_ref, vs_ref, o_ref, *, base):
    length = len_ref[0]
    q = q_ref[...]
    scale = HD ** (-0.5)
    dims = (((1,), (1,)), ((), ()))
    sp = lax.dot_general(q, kp_ref[...], dims, preferred_element_type=jnp.float32) * scale
    ss = lax.dot_general(q, ks_ref[...], dims, preferred_element_type=jnp.float32) * scale
    rows, cols = ss.shape
    qpos = base + lax.broadcasted_iota(jnp.int32, (rows, cols), 0)
    kpos = lax.broadcasted_iota(jnp.int32, (rows, cols), 1)
    allowed = (kpos <= qpos) & (kpos < length)
    ss = jnp.where(allowed, ss, NEG)
    high = jnp.maximum(jnp.max(sp, axis=1, keepdims=True), jnp.max(ss, axis=1, keepdims=True))
    wp = jnp.exp(sp - high)
    ws = jnp.where(allowed, jnp.exp(ss - high), 0.0)
    total = jnp.sum(wp, axis=1, keepdims=True) + jnp.sum(ws, axis=1, keepdims=True)
    acc = jnp.dot(wp.astype(jnp.bfloat16), vp_ref[...], preferred_element_type=jnp.float32)
    acc = acc + jnp.dot(ws.astype(jnp.bfloat16), vs_ref[...], preferred_element_type=jnp.float32)
    o_ref[...] = (acc / total).astype(o_ref.dtype)


def attend(length, query, kp, vp, ks, vs, per_kv, base):
    rows = query.shape[0]
    grid_spec = pltpu.PrefetchScalarGridSpec(
        num_scalar_prefetch=1,
        grid=(per_kv,),
        in_specs=[
            pl.BlockSpec((rows, HD), lambda j, n: (0, j)),
            pl.BlockSpec(kp.shape, lambda j, n: (0, 0)),
            pl.BlockSpec(vp.shape, lambda j, n: (0, 0)),
            pl.BlockSpec(ks.shape, lambda j, n: (0, 0)),
            pl.BlockSpec(vs.shape, lambda j, n: (0, 0)),
        ],
        out_specs=pl.BlockSpec((rows, HD), lambda j, n: (0, j)),
    )
    return pl.pallas_call(
        functools.partial(attention_kernel, base=base),
        grid_spec=grid_spec,
        out_shape=jax.ShapeDtypeStruct((rows, per_kv * HD), jnp.bfloat16),
        compiler_params=pltpu.CompilerParams(vmem_limit_bytes=48 * 1024 * 1024),
        interpret=INTERPRET,
    )(length.reshape(1), query, kp, vp, ks, vs)


def gather_kernel(pages_ref, piece_ref, kv_ref, sem):
    count = pages_ref.shape[0]
    copies = []
    for j in range(count):
        page = pages_ref[j]
        for t in range(2):
            copy = pltpu.make_async_copy(piece_ref.at[page, t], kv_ref.at[t, j], sem.at[t, j])
            copy.start()
            copies.append(copy)
    for copy in copies:
        copy.wait()


def gather_pages(pages, piece):
    count = pages.shape[0]
    out_shape = (2, count) + piece.shape[2:]
    return pl.pallas_call(
        gather_kernel,
        grid_spec=pltpu.PrefetchScalarGridSpec(
            num_scalar_prefetch=1,
            grid=(),
            in_specs=[pl.BlockSpec(memory_space=pl.ANY)],
            out_specs=pl.BlockSpec(memory_space=pl.ANY),
            scratch_shapes=[pltpu.SemaphoreType.DMA((2, count))],
        ),
        out_shape=jax.ShapeDtypeStruct(out_shape, piece.dtype),
        interpret=INTERPRET,
    )(pages, piece)


def shift_perm(n, s):
    return [(j, (j + s) % n) for j in range(n)]


def local(
    hidden_in,
    norm_gain,
    w_query,
    w_key,
    w_value,
    w_out,
    prefix_cache,
    suffix_len,
    page_table,
    request_group,
):
    n_head = lax.axis_size("head")
    me = lax.axis_index("head")
    device = lax.axis_index("tok")
    local_len = hidden_in.shape[1]
    feat = hidden_in.shape[2]
    width = feat * n_head
    chunk = local_len // CHUNKS
    piece = lax.all_gather(prefix_cache, "tok", axis=0, tiled=True)

    x = hidden_in.reshape(local_len, feat)
    recv = []
    for c in range(CHUNKS):
        xc = x[c * chunk:(c + 1) * chunk]
        row = [xc]
        for s in range(1, n_head):
            row.append(lax.ppermute(xc, "head", shift_perm(n_head, s)))
        recv.append(row)

    head_size = HD
    kv_local = w_key.shape[1] // head_size
    q_local = w_query.shape[1] // head_size
    per_kv = q_local // kv_local
    length = suffix_len[device]
    group = request_group[device]
    own_pages = page_table[group]
    kv = gather_pages(own_pages, piece)
    kp = kv[0].reshape(-1, head_size)
    vp = kv[1].reshape(-1, head_size)

    key_chunks = []
    value_chunks = []
    outputs = []
    for c in range(CHUNKS):
        ss = None
        for xb in recv[c]:
            xf = xb.astype(jnp.float32)
            part = jnp.sum(xf * xf, axis=1)
            ss = part if ss is None else ss + part
        inverse = lax.rsqrt(ss / width + EPS)[:, None]
        proj_q = proj_k = proj_v = None
        for s, xb in enumerate(recv[c]):
            src = (me - s) % n_head
            gain = lax.dynamic_slice_in_dim(norm_gain, src * feat, feat)
            nb = (xb.astype(jnp.float32) * inverse * gain[None, :]).astype(jnp.bfloat16)
            pq = jnp.dot(nb, lax.dynamic_slice_in_dim(w_query, src * feat, feat, 0),
                         preferred_element_type=jnp.float32)
            pk = jnp.dot(nb, lax.dynamic_slice_in_dim(w_key, src * feat, feat, 0),
                         preferred_element_type=jnp.float32)
            pv = jnp.dot(nb, lax.dynamic_slice_in_dim(w_value, src * feat, feat, 0),
                         preferred_element_type=jnp.float32)
            if proj_q is None:
                proj_q, proj_k, proj_v = pq, pk, pv
            else:
                proj_q, proj_k, proj_v = proj_q + pq, proj_k + pk, proj_v + pv
        positions = PREFIX + c * chunk + jnp.arange(chunk, dtype=jnp.int32)
        cosine, sine = rope_angles(positions, head_size)
        cosine = cosine[:, None, :]
        sine = sine[:, None, :]
        query = rotate(proj_q.reshape(chunk, q_local, head_size), cosine, sine)
        query = query.astype(jnp.bfloat16).reshape(chunk, q_local * head_size)
        keys = rotate(proj_k.reshape(chunk, kv_local, head_size), cosine, sine)
        key_chunks.append(keys.astype(jnp.bfloat16).reshape(chunk, kv_local * head_size))
        value_chunks.append(proj_v.astype(jnp.bfloat16))
        ks = jnp.concatenate(key_chunks, axis=0) if c else key_chunks[0]
        vs = jnp.concatenate(value_chunks, axis=0) if c else value_chunks[0]
        mixed = attend(length, query, kp, vp, ks, vs, per_kv, c * chunk)

        rows_per = mixed.shape[1]
        output = None
        for s in range(n_head):
            if s == 0:
                part = mixed
            else:
                part = lax.ppermute(mixed, "head", shift_perm(n_head, s))
            src = (me - s) % n_head
            w_rows = lax.dynamic_slice_in_dim(w_out, src * rows_per, rows_per, 0)
            po = jnp.dot(part, w_rows, preferred_element_type=jnp.float32)
            output = po if output is None else output + po
        live = c * chunk + jnp.arange(chunk, dtype=jnp.int32) < length
        outputs.append(jnp.where(live[:, None], output, 0.0).astype(jnp.bfloat16))
    output = jnp.concatenate(outputs, axis=0)
    return output.reshape(1, local_len, w_out.shape[1])


def solution(mesh):
    return jax.shard_map(
        local,
        mesh=mesh,
        in_specs=(
            P("tok", None, "head"),
            P(),
            P(None, "head"),
            P(None, "head"),
            P(None, "head"),
            P(None, "head"),
            P("tok", None, None, "head"),
            P(),
            P(),
            P(),
        ),
        out_specs=P("tok", None, "head"),
        check_vma=False,
    )
```

```python
import functools
import os

import jax
import jax.numpy as jnp
from jax import lax
from jax.experimental import pallas as pl
from jax.experimental.pallas import tpu as pltpu
from jax.sharding import PartitionSpec as P

HD = 128
PREFIX = 4096


THETA = 100000000.0
EPS = 1e-05
NEG = -1e30
TQ = 256
INTERPRET = os.environ.get("SOL_INTERPRET") == "1"


def rope_angles(positions, size):
    half = size // 2
    ladder = jnp.arange(half, dtype=jnp.float32)
    freq = jnp.exp(ladder * (-2.0 * jnp.log(THETA) / size))
    angle = positions.astype(jnp.float32)[:, None] * freq[None, :]
    return (jnp.cos(angle), jnp.sin(angle))


def rotate(values, cosine, sine):
    half = values.shape[-1] // 2
    first = values[..., :half]
    second = values[..., half:]
    return jnp.concatenate(
        [first * cosine - second * sine, second * cosine + first * sine], axis=-1
    )


def attention_kernel(len_ref, pages_ref, q_ref, piece_ref, ks_ref, vs_ref, o_ref, kbuf, vbuf):
    i = pl.program_id(1)

    @pl.when((pl.program_id(0) == 0) & (i == 0))
    def _():
        page = piece_ref.shape[2]
        for j in range(pages_ref.shape[0]):
            slot = pages_ref[j]
            kbuf[j * page:(j + 1) * page, :] = piece_ref[slot, 0]
            vbuf[j * page:(j + 1) * page, :] = piece_ref[slot, 1]

    length = len_ref[0]
    q = q_ref[...]
    scale = HD ** (-0.5)
    dims = (((1,), (1,)), ((), ()))
    sp = lax.dot_general(q, kbuf[...], dims, preferred_element_type=jnp.float32) * scale
    ss = lax.dot_general(q, ks_ref[...], dims, preferred_element_type=jnp.float32) * scale
    rows, cols = ss.shape
    qpos = i * rows + lax.broadcasted_iota(jnp.int32, (rows, cols), 0)
    kpos = lax.broadcasted_iota(jnp.int32, (rows, cols), 1)
    allowed = (kpos <= qpos) & (kpos < length)
    ss = jnp.where(allowed, ss, NEG)
    high = jnp.maximum(jnp.max(sp, axis=1, keepdims=True), jnp.max(ss, axis=1, keepdims=True))
    wp = jnp.exp(sp - high)
    ws = jnp.where(allowed, jnp.exp(ss - high), 0.0)
    total = jnp.sum(wp, axis=1, keepdims=True) + jnp.sum(ws, axis=1, keepdims=True)
    acc = jnp.dot(wp.astype(jnp.bfloat16), vbuf[...], preferred_element_type=jnp.float32)
    acc = acc + jnp.dot(ws.astype(jnp.bfloat16), vs_ref[...], preferred_element_type=jnp.float32)
    o_ref[...] = (acc / total).astype(o_ref.dtype)


def attend(length, pages, query, piece, ks, vs, per_kv):
    local_len = query.shape[0]
    nq = local_len // TQ
    keys_total = pages.shape[0] * piece.shape[2]
    grid_spec = pltpu.PrefetchScalarGridSpec(
        num_scalar_prefetch=2,
        grid=(per_kv, nq),
        in_specs=[
            pl.BlockSpec((TQ, HD), lambda j, i, n, p: (i, j)),
            pl.BlockSpec(piece.shape, lambda j, i, n, p: (0, 0, 0, 0)),
            pl.BlockSpec(ks.shape, lambda j, i, n, p: (0, 0)),
            pl.BlockSpec(vs.shape, lambda j, i, n, p: (0, 0)),
        ],
        out_specs=pl.BlockSpec((TQ, HD), lambda j, i, n, p: (i, j)),
        scratch_shapes=[
            pltpu.VMEM((keys_total, HD), jnp.bfloat16),
            pltpu.VMEM((keys_total, HD), jnp.bfloat16),
        ],
    )
    return pl.pallas_call(
        attention_kernel,
        grid_spec=grid_spec,
        out_shape=jax.ShapeDtypeStruct((local_len, per_kv * HD), jnp.bfloat16),
        compiler_params=pltpu.CompilerParams(vmem_limit_bytes=48 * 1024 * 1024),
        interpret=INTERPRET,
    )(length.reshape(1), pages, query, piece, ks, vs)


def shift_perm(n, s):
    return [(j, (j + s) % n) for j in range(n)]


def rotated_rows(weight, order, blocks):
    rows = weight.shape[0] // blocks
    stacked = weight.reshape(blocks, rows, weight.shape[1])
    return jnp.take(stacked, order, axis=0).reshape(weight.shape)


def local(
    hidden_in,
    norm_gain,
    w_query,
    w_key,
    w_value,
    w_out,
    prefix_cache,
    suffix_len,
    page_table,
    request_group,
):
    n_head = lax.axis_size("head")
    me = lax.axis_index("head")
    device = lax.axis_index("tok")
    local_len = hidden_in.shape[1]
    feat = hidden_in.shape[2]
    piece = lax.all_gather(prefix_cache, "tok", axis=0, tiled=True)

    x = hidden_in.reshape(local_len, feat)
    parts = [x]
    for s in range(1, n_head):
        parts.append(lax.ppermute(x, "head", shift_perm(n_head, s)))
    order = (me - jnp.arange(n_head, dtype=jnp.int32)) % n_head
    gain = rotated_rows(norm_gain.reshape(-1, 1), order, n_head).reshape(-1)
    wq = rotated_rows(w_query, order, n_head)
    wk = rotated_rows(w_key, order, n_head)
    wv = rotated_rows(w_value, order, n_head)
    wo = rotated_rows(w_out, order, n_head)

    flat = jnp.concatenate(parts, axis=1).astype(jnp.float32)
    inverse = lax.rsqrt(jnp.mean(flat * flat, axis=1, keepdims=True) + EPS)
    normed = (flat * inverse * gain[None, :]).astype(jnp.bfloat16)

    head_size = HD
    kv_local = w_key.shape[1] // head_size
    q_local = w_query.shape[1] // head_size
    per_kv = q_local // kv_local
    positions = PREFIX + jnp.arange(local_len, dtype=jnp.int32)
    cosine, sine = rope_angles(positions, head_size)
    cosine = cosine[:, None, :]
    sine = sine[:, None, :]
    query = jnp.dot(normed, wq, preferred_element_type=jnp.float32)
    query = rotate(query.reshape(local_len, q_local, head_size), cosine, sine)
    query = query.astype(jnp.bfloat16).reshape(local_len, q_local * head_size)
    keys = jnp.dot(normed, wk, preferred_element_type=jnp.float32)
    keys = rotate(keys.reshape(local_len, kv_local, head_size), cosine, sine)
    keys = keys.astype(jnp.bfloat16).reshape(local_len, kv_local * head_size)
    values = jnp.dot(normed, wv, preferred_element_type=jnp.float32).astype(jnp.bfloat16)

    length = suffix_len[device]
    group = request_group[device]
    own_pages = page_table[group]
    mixed = attend(length, own_pages, query, piece, keys, values, per_kv)

    gathered = [mixed]
    for s in range(1, n_head):
        gathered.append(lax.ppermute(mixed, "head", shift_perm(n_head, s)))
    output = jnp.dot(jnp.concatenate(gathered, axis=1), wo, preferred_element_type=jnp.float32)
    live = jnp.arange(local_len, dtype=jnp.int32) < length
    output = jnp.where(live[:, None], output, 0.0).astype(jnp.bfloat16)
    return output.reshape(1, local_len, w_out.shape[1])


def solution(mesh):
    return jax.shard_map(
        local,
        mesh=mesh,
        in_specs=(
            P("tok", None, "head"),
            P(),
            P(None, "head"),
            P(None, "head"),
            P(None, "head"),
            P(None, "head"),
            P("tok", None, None, "head"),
            P(),
            P(),
            P(),
        ),
        out_specs=P("tok", None, "head"),
        check_vma=False,
    )
```

```python
import functools
import os

import jax
import jax.numpy as jnp
from jax import lax
from jax.experimental import pallas as pl
from jax.experimental.pallas import tpu as pltpu
from jax.sharding import PartitionSpec as P

HD = 128
PREFIX = 4096


THETA = 100000000.0
EPS = 1e-05
NEG = -1e30
TQ = 256
HALVES = 2
INTERPRET = os.environ.get("SOL_INTERPRET") == "1"


def rope_angles(positions, size):
    half = size // 2
    ladder = jnp.arange(half, dtype=jnp.float32)
    freq = jnp.exp(ladder * (-2.0 * jnp.log(THETA) / size))
    angle = positions.astype(jnp.float32)[:, None] * freq[None, :]
    return (jnp.cos(angle), jnp.sin(angle))


def rotate(values, cosine, sine):
    half = values.shape[-1] // 2
    first = values[..., :half]
    second = values[..., half:]
    return jnp.concatenate(
        [first * cosine - second * sine, second * cosine + first * sine], axis=-1
    )


def attention_kernel(len_ref, pages_ref, q_ref, piece_ref, ks_ref, vs_ref, o_ref, kbuf, vbuf, *, base):
    i = pl.program_id(1)

    @pl.when((pl.program_id(0) == 0) & (i == 0))
    def _():
        page = piece_ref.shape[2]
        for j in range(pages_ref.shape[0]):
            slot = pages_ref[j]
            kbuf[j * page:(j + 1) * page, :] = piece_ref[slot, 0]
            vbuf[j * page:(j + 1) * page, :] = piece_ref[slot, 1]

    length = len_ref[0]
    q = q_ref[...]
    scale = HD ** (-0.5)
    dims = (((1,), (1,)), ((), ()))
    sp = lax.dot_general(q, kbuf[...], dims, preferred_element_type=jnp.float32) * scale
    ss = lax.dot_general(q, ks_ref[...], dims, preferred_element_type=jnp.float32) * scale
    rows, cols = ss.shape
    qpos = base + i * rows + lax.broadcasted_iota(jnp.int32, (rows, cols), 0)
    kpos = lax.broadcasted_iota(jnp.int32, (rows, cols), 1)
    allowed = (kpos <= qpos) & (kpos < length)
    ss = jnp.where(allowed, ss, NEG)
    high = jnp.maximum(jnp.max(sp, axis=1, keepdims=True), jnp.max(ss, axis=1, keepdims=True))
    wp = jnp.exp(sp - high)
    ws = jnp.where(allowed, jnp.exp(ss - high), 0.0)
    total = jnp.sum(wp, axis=1, keepdims=True) + jnp.sum(ws, axis=1, keepdims=True)
    acc = jnp.dot(wp.astype(jnp.bfloat16), vbuf[...], preferred_element_type=jnp.float32)
    acc = acc + jnp.dot(ws.astype(jnp.bfloat16), vs_ref[...], preferred_element_type=jnp.float32)
    o_ref[...] = (acc / total).astype(o_ref.dtype)


def attend(length, pages, query, piece, ks, vs, per_kv, base):
    local_len = query.shape[0]
    nq = local_len // TQ
    keys_total = pages.shape[0] * piece.shape[2]
    grid_spec = pltpu.PrefetchScalarGridSpec(
        num_scalar_prefetch=2,
        grid=(per_kv, nq),
        in_specs=[
            pl.BlockSpec((TQ, HD), lambda j, i, n, p: (i, j)),
            pl.BlockSpec(piece.shape, lambda j, i, n, p: (0, 0, 0, 0)),
            pl.BlockSpec(ks.shape, lambda j, i, n, p: (0, 0)),
            pl.BlockSpec(vs.shape, lambda j, i, n, p: (0, 0)),
        ],
        out_specs=pl.BlockSpec((TQ, HD), lambda j, i, n, p: (i, j)),
        scratch_shapes=[
            pltpu.VMEM((keys_total, HD), jnp.bfloat16),
            pltpu.VMEM((keys_total, HD), jnp.bfloat16),
        ],
    )
    return pl.pallas_call(
        functools.partial(attention_kernel, base=base),
        grid_spec=grid_spec,
        out_shape=jax.ShapeDtypeStruct((local_len, per_kv * HD), jnp.bfloat16),
        compiler_params=pltpu.CompilerParams(vmem_limit_bytes=48 * 1024 * 1024),
        interpret=INTERPRET,
    )(length.reshape(1), pages, query, piece, ks, vs)


def shift_perm(n, s):
    return [(j, (j + s) % n) for j in range(n)]


def rotated_rows(weight, order, blocks):
    rows = weight.shape[0] // blocks
    stacked = weight.reshape(blocks, rows, weight.shape[1])
    return jnp.take(stacked, order, axis=0).reshape(weight.shape)


def local(
    hidden_in,
    norm_gain,
    w_query,
    w_key,
    w_value,
    w_out,
    prefix_cache,
    suffix_len,
    page_table,
    request_group,
):
    n_head = lax.axis_size("head")
    me = lax.axis_index("head")
    device = lax.axis_index("tok")
    local_len = hidden_in.shape[1]
    feat = hidden_in.shape[2]
    piece = lax.all_gather(prefix_cache, "tok", axis=0, tiled=True)

    x = hidden_in.reshape(local_len, feat)
    parts = [x]
    for s in range(1, n_head):
        parts.append(lax.ppermute(x, "head", shift_perm(n_head, s)))
    order = (me - jnp.arange(n_head, dtype=jnp.int32)) % n_head
    gain = rotated_rows(norm_gain.reshape(-1, 1), order, n_head).reshape(-1)
    q_cols = w_query.shape[1]
    kv_cols = w_key.shape[1]
    w_all = jnp.concatenate([w_query, w_key, w_value], axis=1)
    w_all = rotated_rows(w_all, order, n_head)
    wo = rotated_rows(w_out, order, n_head)

    flat = jnp.concatenate(parts, axis=1).astype(jnp.float32)
    inverse = lax.rsqrt(jnp.mean(flat * flat, axis=1, keepdims=True) + EPS)
    normed = (flat * inverse * gain[None, :]).astype(jnp.bfloat16)

    head_size = HD
    kv_local = kv_cols // head_size
    q_local = q_cols // head_size
    per_kv = q_local // kv_local
    positions = PREFIX + jnp.arange(local_len, dtype=jnp.int32)
    cosine, sine = rope_angles(positions, head_size)
    cosine = cosine[:, None, :]
    sine = sine[:, None, :]
    projected = jnp.dot(normed, w_all, preferred_element_type=jnp.float32)
    query = projected[:, :q_cols]
    query = rotate(query.reshape(local_len, q_local, head_size), cosine, sine)
    query = query.astype(jnp.bfloat16).reshape(local_len, q_local * head_size)
    keys = projected[:, q_cols:q_cols + kv_cols]
    keys = rotate(keys.reshape(local_len, kv_local, head_size), cosine, sine)
    keys = keys.astype(jnp.bfloat16).reshape(local_len, kv_local * head_size)
    values = projected[:, q_cols + kv_cols:].astype(jnp.bfloat16)

    length = suffix_len[device]
    group = request_group[device]
    own_pages = page_table[group]
    half = local_len // HALVES
    outputs = []
    for c in range(HALVES):
        lo, hi = c * half, (c + 1) * half
        mixed = attend(length, own_pages, query[lo:hi], piece, keys[:hi], values[:hi],
                       per_kv, lo)
        gathered = [mixed]
        for s in range(1, n_head):
            gathered.append(lax.ppermute(mixed, "head", shift_perm(n_head, s)))
        output = jnp.dot(jnp.concatenate(gathered, axis=1), wo,
                         preferred_element_type=jnp.float32)
        live = lo + jnp.arange(half, dtype=jnp.int32) < length
        outputs.append(jnp.where(live[:, None], output, 0.0).astype(jnp.bfloat16))
    output = jnp.concatenate(outputs, axis=0)
    return output.reshape(1, local_len, w_out.shape[1])


def solution(mesh):
    return jax.shard_map(
        local,
        mesh=mesh,
        in_specs=(
            P("tok", None, "head"),
            P(),
            P(None, "head"),
            P(None, "head"),
            P(None, "head"),
            P(None, "head"),
            P("tok", None, None, "head"),
            P(),
            P(),
            P(),
        ),
        out_specs=P("tok", None, "head"),
        check_vma=False,
    )
```
